256 devices in a mesh: sample: 16 (over y_hi, z), space: 16 (over y_lo, x, core).
Axes of the slice: x: 4, y: 4 (y_hi: 2, y_lo: 2; y = y_hi * 2 + y_lo), z: 8, core: 2. Of those that a mesh axis runs over, the one named last changes fastest.
Arguments:
- volumes: bfloat16 [16, 32, 64, 1024], P('sample', None, 'space'), may hold values from -6 to 6
- first_weight: bfloat16 [64, 864], replicated, may hold values from -0.21875 to 0.21875
- first_bias: float32 [64], replicated, may hold values from -3 to 3
- second_weight: bfloat16 [128, 1728], replicated, may hold values from -0.15625 to 0.15625
- second_bias: float32 [128], replicated, may hold values from -3 to 3
- cotangent: bfloat16 [16, 128, 32, 256], P('sample', None, 'space'), may hold values from -6 to 6
Outputs:
- activation: bfloat16 [16, 128, 32, 256], P('sample', None, 'space')
- input_grad: bfloat16 [16, 32, 64, 1024], P('sample', None, 'space')
- first_wgrad: float32 [64, 864], replicated
- first_bgrad: float32 [64], replicated
- second_wgrad: float32 [128, 1728], replicated
- second_bgrad: float32 [128], replicated
The draws below stay inside these ranges and needn't reach their ends.
All inputs are finite; a program needn't handle non-finite values.
Results may differ from the reference program's by a relative error of at most 0.013.
Values may be sent and summed in bfloat16 or wider, within the bound.
No kernel may reach another device: no remote copies, remote signals or barrier semaphores. Data moves between devices by JAX's collectives and lax.ppermute only.
A program may use at most 64 MiB of HBM per device.

```python
import math
import jax
import jax.numpy as jnp
from jax import lax

CH_IN = 32
CH_MID = 64
CH_OUT = 128
VOL_DEPTH = 64
VOL_HEIGHT = 64
VOL_WIDTH = 16
SAMPLES = 16
PLANE = 1024


def block_levels(rng, shape, split, low, largest):
    def one(position, parts):
        draws = jax.random.uniform(jax.random.fold_in(jax.random.fold_in(rng, 6), position), (parts,), jnp.float32, low / len(split), largest / len(split))
        return jnp.repeat(jnp.exp(draws), shape[position] // parts).reshape((-1,) + (1,) * (len(shape) - position - 1))

    loudness = one(*split[0])
    for cut in split[1:]:
        loudness = loudness * one(*cut)
    return loudness


def centred(own_key, extent, spread, reach, split=(), dtype=jnp.bfloat16):
    values = jax.random.normal(own_key, extent, jnp.float32) * spread
    if len(split) > 0:
        values = block_levels(own_key, extent, split, -0.22, 0.18) * values
    return jnp.clip(values, min=-reach, max=reach).astype(dtype)


def setup_inputs(seed: int = 0) -> dict:
    splits = jax.random.split(jax.random.key(seed), 7)
    volumes = centred(splits[0], (SAMPLES, CH_IN, VOL_DEPTH, PLANE), 1.0, 6.0, ((0, 16), (2, 16)))
    first_weight = centred(splits[1], (CH_MID, 27 * CH_IN), (27 * CH_IN) ** -0.5, 0.21875)
    first_bias = centred(splits[2], (CH_MID,), 0.5, 3.0, (), jnp.float32)
    second_weight = centred(splits[3], (CH_OUT, 27 * CH_MID), (27 * CH_MID) ** -0.5, 0.15625)
    second_bias = centred(splits[4], (CH_OUT,), 0.5, 3.0, (), jnp.float32)
    cotangent = centred(splits[5], (SAMPLES, CH_OUT, VOL_DEPTH // 2, PLANE // 4), 1.0, 6.0, ((0, 16), (2, 16)))
    return {"volumes": volumes, "first_weight": first_weight, "first_bias": first_bias, "second_weight": second_weight, "second_bias": second_bias, "cotangent": cotangent}


LAYOUT_SPEC = ('NCDHW', 'OIDHW', 'NCDHW')

def kernel_of(weight, channels):
    return weight.astype(jnp.float32).reshape(weight.shape[0], 3, 3, 3, channels).transpose(0, 4, 1, 2, 3)

def flipped(kernel):
    return jnp.flip(kernel, (2, 3, 4)).transpose(1, 0, 2, 3, 4)

def correlate(padded, kernel):
    return lax.conv_general_dilated(padded, kernel, (1, 1, 1), 'VALID', dimension_numbers=LAYOUT_SPEC, precision=lax.Precision.HIGHEST)

def pad_all(volume):
    return jnp.pad(volume, ((0, 0), (0, 0), (1, 1), (1, 1), (1, 1)))

def silu_slope(values_in):
    sigmoid_v = jax.nn.sigmoid(values_in)
    return sigmoid_v * (1.0 + values_in * (1.0 - sigmoid_v))

def upsampled(pooled_grad, slope):
    sample_count, channels, planes, rows_half, cols_half = pooled_grad.shape
    shaped = slope.reshape(sample_count, channels, planes, 2, rows_half, 2, cols_half, 2)
    return (pooled_grad[:, :, :, None, :, None, :, None] * 0.125 * shaped).reshape(slope.shape)

def weight_grad(padded, slope_grad):
    depth_cells, height_cells, width_cells = slope_grad.shape[2:]
    columns = []
    for offset in range(27):
        depth_off, height_off, width_off = (offset // 9, offset // 3 % 3, offset % 3)
        window = padded[:, :, depth_off:depth_off + depth_cells, height_off:height_off + height_cells, width_off:width_off + width_cells]
        columns.append(lax.dot_general(slope_grad, window, (((0, 2, 3, 4), (0, 2, 3, 4)), ((), ())), precision=lax.Precision.HIGHEST))
    return jnp.concatenate(columns, axis=1)

def one_sample(volume, cot_sample, first_weight, first_bias, second_weight, second_bias):
    inputs = volume.astype(jnp.float32).reshape(1, CH_IN, VOL_DEPTH, VOL_HEIGHT, VOL_WIDTH)
    kernel_one = kernel_of(first_weight, CH_IN)
    kernel_two = kernel_of(second_weight, CH_MID)
    padded_in = pad_all(inputs)
    first_pre = correlate(padded_in, kernel_one) + first_bias.reshape(1, CH_MID, 1, 1, 1)
    pooled = jax.nn.silu(first_pre).reshape(1, CH_MID, VOL_DEPTH // 2, 2, VOL_HEIGHT // 2, 2, VOL_WIDTH // 2, 2).mean(axis=(3, 5, 7)).astype(jnp.bfloat16)
    padded_pool = pad_all(pooled.astype(jnp.float32))
    second_pre = correlate(padded_pool, kernel_two) + second_bias.reshape(1, CH_OUT, 1, 1, 1)
    activation = jax.nn.silu(second_pre).astype(jnp.bfloat16)
    cot_cells = cot_sample.astype(jnp.float32).reshape(1, CH_OUT, VOL_DEPTH // 2, VOL_HEIGHT // 2, VOL_WIDTH // 2)
    second_grad = (cot_cells * silu_slope(second_pre)).astype(jnp.bfloat16).astype(jnp.float32)
    pooled_grad = correlate(pad_all(second_grad), flipped(kernel_two))
    first_grad = upsampled(pooled_grad, silu_slope(first_pre)).astype(jnp.bfloat16).astype(jnp.float32)
    input_grad = correlate(pad_all(first_grad), flipped(kernel_one)).astype(jnp.bfloat16)
    return (activation.reshape(CH_OUT, VOL_DEPTH // 2, PLANE // 4), input_grad.reshape(CH_IN, VOL_DEPTH, PLANE), weight_grad(padded_in, first_grad), lax.optimization_barrier(jnp.sum(first_grad, axis=(0, 2, 3, 4))), weight_grad(padded_pool, second_grad), lax.optimization_barrier(jnp.sum(second_grad, axis=(0, 2, 3, 4))))

def reference(volumes, first_weight, first_bias, second_weight, second_bias, cotangent):

    def one_step(sample_pair):
        return one_sample(sample_pair[0], sample_pair[1], first_weight, first_bias, second_weight, second_bias)
    results = lax.map(one_step, (volumes, cotangent))
    factor = 1.0 / math.sqrt(SAMPLES * VOL_DEPTH * VOL_HEIGHT * VOL_WIDTH / 8.0)
    return (results[0], results[1], lax.optimization_barrier(jnp.sum(results[2], axis=0)) * factor, lax.optimization_barrier(jnp.sum(results[3], axis=0)) * factor, lax.optimization_barrier(jnp.sum(results[4], axis=0)) * factor, lax.optimization_barrier(jnp.sum(results[5], axis=0)) * factor)
```

```python
import math

import jax
import jax.numpy as jnp
from jax import lax
from jax.sharding import PartitionSpec as P

CH_IN = 32
CH_MID = 64
CH_OUT = 128
VOL_HEIGHT = 64
VOL_WIDTH = 16


LAYOUT_SPEC = ("NCDHW", "OIDHW", "NCDHW")


def padded_2(x, sides, width):
    for axis, dim in sides:
        size, length = (lax.axis_size(axis), x.shape[dim])
        up = [(i, (i + 1) % size) for i in range(size - 1)]
        down = [(j, i) for i, j in up]
        last = lax.slice_in_dim(x, length - width, length, axis=dim)
        initial = lax.slice_in_dim(x, 0, width, axis=dim)
        before = lax.ppermute(last, axis, up)
        after = lax.ppermute(initial, axis, down)
        x = jnp.concatenate([before, x, after], axis=dim)
    return x


def from_partner(block, axis, stride):
    count = lax.axis_size(axis)
    route = []
    for low in range(count):
        high = low | 1 << stride
        if high != low and high < count:
            route += [(low, high), (high, low)]
    return lax.ppermute(block, axis, route)


def shifted(x, axis, by):
    size = lax.axis_size(axis)
    pairs = [(i, i + by) for i in range(size) if 0 <= i + by < size]
    return lax.ppermute(x, axis, pairs)


def as_sent(x):

    def short(part):
        return part.astype(jnp.bfloat16) if part.dtype == jnp.float32 else part

    return jax.tree.map(short, x)


def kernel_of(weight, channels):
    return weight.reshape(weight.shape[0], 3, 3, 3, channels).transpose(0, 4, 1, 2, 3)


def flipped(kernel):
    return jnp.flip(kernel, (2, 3, 4)).transpose(1, 0, 2, 3, 4)


def correlate(padded, kernel):
    return lax.conv_general_dilated(
        padded,
        kernel,
        (1, 1, 1),
        "VALID",
        dimension_numbers=LAYOUT_SPEC,
        preferred_element_type=jnp.float32,
    )


def pad_sides(volume, depth_pad, height_pad):
    return jnp.pad(
        volume, ((0, 0), (0, 0), (depth_pad, depth_pad), (height_pad, height_pad), (1, 1))
    )


def silu_slope(values_in):
    sigmoid_v = jax.nn.sigmoid(values_in)
    return sigmoid_v * (1.0 + values_in * (1.0 - sigmoid_v))


def upsampled(pooled_grad, slope):
    sample_count, channels, planes, rows_half, cols_half = pooled_grad.shape
    shaped = slope.reshape(sample_count, channels, planes, 2, rows_half, 2, cols_half, 2)
    return (pooled_grad[:, :, :, None, :, None, :, None] * 0.125 * shaped).reshape(slope.shape)


def weight_grad(padded, slope_grad):
    depth_cells, height_cells, width_cells = slope_grad.shape[2:]
    columns = []
    for offset in range(27):
        depth_off, height_off, width_off = (offset // 9, offset // 3 % 3, offset % 3)
        window = padded[
            :,
            :,
            depth_off : depth_off + depth_cells,
            height_off : height_off + height_cells,
            width_off : width_off + width_cells,
        ]
        columns.append(
            lax.dot_general(
                slope_grad,
                window,
                (((0, 2, 3, 4), (0, 2, 3, 4)), ((), ())),
                preferred_element_type=jnp.float32,
            )
        )
    return jnp.concatenate(columns, axis=1)


def butterfly(pieces_all, mover, own_index, bit_levels):
    for bit_level in range(bit_levels):
        step_size = 1 << bit_level
        outer_count = pieces_all.shape[0] // (2 * step_size)
        trailing = pieces_all.shape[1:]
        grouped = pieces_all.reshape((outer_count, 2, step_size) + trailing)
        lower_half = grouped[:, 0]
        upper_half = grouped[:, 1]
        bit_set = own_index >> bit_level & 1 == 1
        kept_half = jnp.where(bit_set, upper_half, lower_half)
        sent_half = jnp.where(bit_set, lower_half, upper_half)
        arrived = mover(sent_half, bit_level)
        new_lower = jnp.where(bit_set, arrived, kept_half)
        new_upper = jnp.where(bit_set, kept_half, arrived)
        pieces_all = jnp.stack([new_lower, new_upper], axis=1).reshape(pieces_all.shape)
    return pieces_all


def slabs_to_blocks(slab, mover, own_index, block_side, bit_levels):
    sample_count, channels, planes, rows_all, row_cells = slab.shape
    rows_block = rows_all // block_side
    pieces_all = jnp.moveaxis(
        slab.reshape(sample_count, channels, planes, block_side, rows_block * row_cells), 3, 0
    )
    arrived = jnp.moveaxis(butterfly(pieces_all, mover, own_index, bit_levels), 0, 2)
    return arrived.reshape(sample_count, channels, block_side * planes, rows_block, row_cells)


def blocks_to_slabs(block, mover, own_index, block_side, bit_levels):
    sample_count, channels, planes_all, rows_block, row_cells = block.shape
    planes = planes_all // block_side
    pieces_all = jnp.moveaxis(
        block.reshape(sample_count, channels, block_side, planes, rows_block * row_cells), 2, 0
    )
    arrived = jnp.moveaxis(butterfly(pieces_all, mover, own_index, bit_levels), 0, 3)
    return arrived.reshape(sample_count, channels, planes, block_side * rows_block * row_cells)


def block_halo(block, movers, own_index, block_side):
    sample_count, channels, planes, rows_block, row_cells = block.shape
    block_column = own_index % block_side
    last_row = block[:, :, :, rows_block - 1].reshape(sample_count, channels, planes * row_cells)
    first_row = block[:, :, :, 0].reshape(sample_count, channels, planes * row_cells)
    last_row = jnp.where(block_column == block_side - 1, jnp.zeros_like(last_row), last_row)
    first_row = jnp.where(block_column == 0, jnp.zeros_like(first_row), first_row)
    from_prev = movers[0](last_row)
    from_next = movers[1](first_row)
    tall_block = jnp.concatenate(
        [
            from_prev.reshape(sample_count, channels, planes, 1, row_cells),
            block,
            from_next.reshape(sample_count, channels, planes, 1, row_cells),
        ],
        axis=3,
    )
    top_plane = tall_block[:, :, planes - 1].reshape(
        sample_count, channels, (rows_block + 2) * row_cells
    )
    bottom_plane = tall_block[:, :, 0].reshape(sample_count, channels, (rows_block + 2) * row_cells)
    from_below = movers[2](top_plane)
    from_above = movers[3](bottom_plane)
    full_block = jnp.concatenate(
        [
            from_below.reshape(sample_count, channels, 1, rows_block + 2, row_cells),
            tall_block,
            from_above.reshape(sample_count, channels, 1, rows_block + 2, row_cells),
        ],
        axis=2,
    )
    return jnp.pad(full_block, ((0, 0), (0, 0), (0, 0), (0, 0), (1, 1)))


def all_summed(parts, axes):
    flat = jnp.concatenate([part.reshape(-1) for part in parts])
    levels = []
    for axis in axes:
        for bit in range(lax.axis_size(axis).bit_length() - 1):
            levels.append((axis, bit))
    block = 1 << len(levels)
    total = flat.shape[0]
    current = jnp.pad(flat, (0, -total % block))
    for axis, bit in levels:
        half = current.shape[0] // 2
        upper = (lax.axis_index(axis) >> bit & 1) == 1
        kept = jnp.where(upper, current[half:], current[:half])
        sent = jnp.where(upper, current[:half], current[half:])
        pairs = [(i, i ^ 1 << bit) for i in range(lax.axis_size(axis))]
        current = kept + lax.ppermute(sent, axis, pairs)
    for axis, bit in reversed(levels):
        upper = (lax.axis_index(axis) >> bit & 1) == 1
        pairs = [(i, i ^ 1 << bit) for i in range(lax.axis_size(axis))]
        other = lax.ppermute(current, axis, pairs)
        current = jnp.where(
            upper, jnp.concatenate([other, current]), jnp.concatenate([current, other])
        )
    results, start = [], 0
    for part in parts:
        results.append(current[start : start + part.size].reshape(part.shape))
        start += part.size
    return tuple(results)


def per_device(volumes, first_weight, first_bias, second_weight, second_bias, cotangent):
    sample_count = volumes.shape[0]
    depth_cells = volumes.shape[2]
    plane_cells = volumes.shape[3]
    space_count = lax.axis_size("space")
    total_samples = sample_count * lax.axis_size("sample")
    half_height = VOL_HEIGHT // 2
    half_width = VOL_WIDTH // 2
    pooled_planes = depth_cells // 2
    grad_scale = 1.0 / math.sqrt(
        total_samples * depth_cells * space_count * VOL_HEIGHT * VOL_WIDTH / 8.0
    )
    kernel_one = kernel_of(first_weight, CH_IN)
    kernel_two = kernel_of(second_weight, CH_MID)
    haloed_in = padded_2(volumes, (("space", 2),), 1)
    padded_in = pad_sides(
        haloed_in.reshape(sample_count, CH_IN, depth_cells + 2, VOL_HEIGHT, VOL_WIDTH), 0, 1
    )
    first_pre = correlate(padded_in, kernel_one) + first_bias.reshape(1, CH_MID, 1, 1, 1)
    pooled = (
        jax.nn.silu(first_pre)
        .reshape(sample_count, CH_MID, pooled_planes, 2, half_height, 2, half_width, 2)
        .mean(axis=(3, 5, 7))
        .astype(jnp.bfloat16)
    )
    cot_cells = cotangent.reshape(sample_count, CH_OUT, pooled_planes, half_height, half_width)
    own_index = lax.axis_index("space")
    block_side = math.isqrt(space_count)
    bit_levels = block_side.bit_length() - 1
    pooled_block = slabs_to_blocks(
        pooled,
        lambda piece_in, bit_level: from_partner(piece_in, "space", bit_level),
        own_index,
        block_side,
        bit_levels,
    )
    cot_block = slabs_to_blocks(
        cot_cells,
        lambda piece_in, bit_level: from_partner(piece_in, "space", bit_level),
        own_index,
        block_side,
        bit_levels,
    )
    pooled_movers = (
        lambda piece_in: shifted(piece_in, "space", 1),
        lambda piece_in: shifted(piece_in, "space", -1),
        lambda piece_in: shifted(piece_in, "space", block_side),
        lambda piece_in: shifted(piece_in, "space", -block_side),
    )
    padded_pool = block_halo(pooled_block, pooled_movers, own_index, block_side)
    second_pre = correlate(padded_pool, kernel_two) + second_bias.reshape(1, CH_OUT, 1, 1, 1)
    second_grad = (cot_block.astype(jnp.float32) * silu_slope(second_pre)).astype(jnp.bfloat16)
    grad_movers = (
        lambda piece_in: shifted(piece_in, "space", 1),
        lambda piece_in: shifted(piece_in, "space", -1),
        lambda piece_in: shifted(piece_in, "space", block_side),
        lambda piece_in: shifted(piece_in, "space", -block_side),
    )
    padded_grad = block_halo(second_grad, grad_movers, own_index, block_side)
    grad_block = correlate(padded_grad, flipped(kernel_two))
    activation = blocks_to_slabs(
        jax.nn.silu(second_pre).astype(jnp.bfloat16),
        lambda piece_in, bit_level: from_partner(piece_in, "space", bit_level),
        own_index,
        block_side,
        bit_levels,
    )
    pooled_grad = blocks_to_slabs(
        grad_block,
        lambda piece_in, bit_level: from_partner(as_sent(piece_in), "space", bit_level).astype(
            piece_in.dtype
        ),
        own_index,
        block_side,
        bit_levels,
    )
    second_wgrad = weight_grad(padded_pool, second_grad)
    second_bgrad = jnp.sum(second_grad, axis=(0, 2, 3, 4), dtype=jnp.float32)
    pooled_cells = pooled_grad.reshape(sample_count, CH_MID, pooled_planes, half_height, half_width)
    first_grad = upsampled(pooled_cells, silu_slope(first_pre)).astype(jnp.bfloat16)
    first_wgrad = weight_grad(padded_in, first_grad)
    first_bgrad = jnp.sum(first_grad, axis=(0, 2, 3, 4), dtype=jnp.float32)
    first_wgrad, first_bgrad, second_wgrad, second_bgrad = all_summed(
        (first_wgrad, first_bgrad, second_wgrad, second_bgrad), ("space", "sample")
    )
    flip_one = flipped(kernel_one)
    haloed_grad = padded_2(
        first_grad.reshape(sample_count, CH_MID, depth_cells, plane_cells), (("space", 2),), 1
    )
    input_sum = correlate(
        pad_sides(
            haloed_grad.reshape(sample_count, CH_MID, depth_cells + 2, VOL_HEIGHT, VOL_WIDTH), 0, 1
        ),
        flip_one,
    )
    input_sum = input_sum.reshape(sample_count, CH_IN, depth_cells, plane_cells)
    input_grad = input_sum.astype(jnp.bfloat16)
    return (
        activation,
        input_grad,
        first_wgrad * grad_scale,
        first_bgrad * grad_scale,
        second_wgrad * grad_scale,
        second_bgrad * grad_scale,
    )


def solution(mesh):
    in_specs = (
        P("sample", None, "space", None),
        P(),
        P(),
        P(),
        P(),
        P("sample", None, "space", None),
    )
    out_specs = (
        P("sample", None, "space", None),
        P("sample", None, "space", None),
        P(),
        P(),
        P(),
        P(),
    )
    return jax.shard_map(
        per_device, mesh=mesh, in_specs=in_specs, out_specs=out_specs, check_vma=False
    )
```

```python
import math

import jax
import jax.numpy as jnp
from jax import lax
from jax.sharding import PartitionSpec as P

CH_IN = 32
CH_MID = 64
CH_OUT = 128
VOL_HEIGHT = 64
VOL_WIDTH = 16


LAYOUT_SPEC = ("NCDHW", "OIDHW", "NCDHW")


def padded_2(x, sides, width):
    for axis, dim in sides:
        size, length = (lax.axis_size(axis), x.shape[dim])
        up = [(i, (i + 1) % size) for i in range(size - 1)]
        down = [(j, i) for i, j in up]
        last = lax.slice_in_dim(x, length - width, length, axis=dim)
        initial = lax.slice_in_dim(x, 0, width, axis=dim)
        before = lax.ppermute(last, axis, up)
        after = lax.ppermute(initial, axis, down)
        x = jnp.concatenate([before, x, after], axis=dim)
    return x


def from_partner(block, axis, stride):
    count = lax.axis_size(axis)
    route = []
    for low in range(count):
        high = low | 1 << stride
        if high != low and high < count:
            route += [(low, high), (high, low)]
    return lax.ppermute(block, axis, route)


def shifted(x, axis, by):
    size = lax.axis_size(axis)
    pairs = [(i, i + by) for i in range(size) if 0 <= i + by < size]
    return lax.ppermute(x, axis, pairs)


def as_sent(x):

    def short(part):
        return part.astype(jnp.bfloat16) if part.dtype == jnp.float32 else part

    return jax.tree.map(short, x)


def kernel_of(weight, channels):
    return weight.reshape(weight.shape[0], 3, 3, 3, channels).transpose(0, 4, 1, 2, 3)


def flipped(kernel):
    return jnp.flip(kernel, (2, 3, 4)).transpose(1, 0, 2, 3, 4)


def correlate(padded, kernel):
    return lax.conv_general_dilated(
        padded,
        kernel,
        (1, 1, 1),
        "VALID",
        dimension_numbers=LAYOUT_SPEC,
        preferred_element_type=jnp.float32,
    )


def pad_sides(volume, depth_pad, height_pad):
    return jnp.pad(
        volume, ((0, 0), (0, 0), (depth_pad, depth_pad), (height_pad, height_pad), (1, 1))
    )


def silu_slope(values_in):
    sigmoid_v = jax.nn.sigmoid(values_in)
    return sigmoid_v * (1.0 + values_in * (1.0 - sigmoid_v))


def upsampled(pooled_grad, slope):
    sample_count, channels, planes, rows_half, cols_half = pooled_grad.shape
    shaped = slope.reshape(sample_count, channels, planes, 2, rows_half, 2, cols_half, 2)
    return (pooled_grad[:, :, :, None, :, None, :, None] * 0.125 * shaped).reshape(slope.shape)


def weight_grad(padded, slope_grad):
    summed = lax.conv_general_dilated(
        padded,
        slope_grad,
        (1, 1, 1),
        "VALID",
        dimension_numbers=("CNDHW", "IODHW", "CNDHW"),
        preferred_element_type=jnp.float32,
    )
    out_channels, in_channels = summed.shape[:2]
    return summed.transpose(0, 2, 3, 4, 1).reshape(out_channels, 27 * in_channels)


def butterfly(pieces_all, mover, own_index, bit_levels):
    for bit_level in range(bit_levels):
        step_size = 1 << bit_level
        outer_count = pieces_all.shape[0] // (2 * step_size)
        trailing = pieces_all.shape[1:]
        grouped = pieces_all.reshape((outer_count, 2, step_size) + trailing)
        lower_half = grouped[:, 0]
        upper_half = grouped[:, 1]
        bit_set = own_index >> bit_level & 1 == 1
        kept_half = jnp.where(bit_set, upper_half, lower_half)
        sent_half = jnp.where(bit_set, lower_half, upper_half)
        arrived = mover(sent_half, bit_level)
        new_lower = jnp.where(bit_set, arrived, kept_half)
        new_upper = jnp.where(bit_set, kept_half, arrived)
        pieces_all = jnp.stack([new_lower, new_upper], axis=1).reshape(pieces_all.shape)
    return pieces_all


def slabs_to_blocks(slab, mover, own_index, block_side, bit_levels):
    sample_count, channels, planes, rows_all, row_cells = slab.shape
    rows_block = rows_all // block_side
    pieces_all = jnp.moveaxis(
        slab.reshape(sample_count, channels, planes, block_side, rows_block * row_cells), 3, 0
    )
    arrived = jnp.moveaxis(butterfly(pieces_all, mover, own_index, bit_levels), 0, 2)
    return arrived.reshape(sample_count, channels, block_side * planes, rows_block, row_cells)


def blocks_to_slabs(block, mover, own_index, block_side, bit_levels):
    sample_count, channels, planes_all, rows_block, row_cells = block.shape
    planes = planes_all // block_side
    pieces_all = jnp.moveaxis(
        block.reshape(sample_count, channels, block_side, planes, rows_block * row_cells), 2, 0
    )
    arrived = jnp.moveaxis(butterfly(pieces_all, mover, own_index, bit_levels), 0, 3)
    return arrived.reshape(sample_count, channels, planes, block_side * rows_block * row_cells)


def block_halo(block, movers, own_index, block_side):
    sample_count, channels, planes, rows_block, row_cells = block.shape
    block_column = own_index % block_side
    last_row = block[:, :, :, rows_block - 1].reshape(sample_count, channels, planes * row_cells)
    first_row = block[:, :, :, 0].reshape(sample_count, channels, planes * row_cells)
    last_row = jnp.where(block_column == block_side - 1, jnp.zeros_like(last_row), last_row)
    first_row = jnp.where(block_column == 0, jnp.zeros_like(first_row), first_row)
    from_prev = movers[0](last_row)
    from_next = movers[1](first_row)
    tall_block = jnp.concatenate(
        [
            from_prev.reshape(sample_count, channels, planes, 1, row_cells),
            block,
            from_next.reshape(sample_count, channels, planes, 1, row_cells),
        ],
        axis=3,
    )
    top_plane = tall_block[:, :, planes - 1].reshape(
        sample_count, channels, (rows_block + 2) * row_cells
    )
    bottom_plane = tall_block[:, :, 0].reshape(sample_count, channels, (rows_block + 2) * row_cells)
    from_below = movers[2](top_plane)
    from_above = movers[3](bottom_plane)
    full_block = jnp.concatenate(
        [
            from_below.reshape(sample_count, channels, 1, rows_block + 2, row_cells),
            tall_block,
            from_above.reshape(sample_count, channels, 1, rows_block + 2, row_cells),
        ],
        axis=2,
    )
    return jnp.pad(full_block, ((0, 0), (0, 0), (0, 0), (0, 0), (1, 1)))


def all_summed(parts, axes):
    flat = jnp.concatenate([part.reshape(-1) for part in parts])
    levels = []
    for axis in axes:
        for bit in range(lax.axis_size(axis).bit_length() - 1):
            levels.append((axis, bit))
    block = 1 << len(levels)
    total = flat.shape[0]
    current = jnp.pad(flat, (0, -total % block))
    for axis, bit in levels:
        half = current.shape[0] // 2
        upper = (lax.axis_index(axis) >> bit & 1) == 1
        kept = jnp.where(upper, current[half:], current[:half])
        sent = jnp.where(upper, current[:half], current[half:])
        pairs = [(i, i ^ 1 << bit) for i in range(lax.axis_size(axis))]
        current = kept + lax.ppermute(sent, axis, pairs)
    for axis, bit in reversed(levels):
        upper = (lax.axis_index(axis) >> bit & 1) == 1
        pairs = [(i, i ^ 1 << bit) for i in range(lax.axis_size(axis))]
        other = lax.ppermute(current, axis, pairs)
        current = jnp.where(
            upper, jnp.concatenate([other, current]), jnp.concatenate([current, other])
        )
    results, start = [], 0
    for part in parts:
        results.append(current[start : start + part.size].reshape(part.shape))
        start += part.size
    return tuple(results)


def per_device(volumes, first_weight, first_bias, second_weight, second_bias, cotangent):
    sample_count = volumes.shape[0]
    depth_cells = volumes.shape[2]
    plane_cells = volumes.shape[3]
    space_count = lax.axis_size("space")
    total_samples = sample_count * lax.axis_size("sample")
    half_height = VOL_HEIGHT // 2
    half_width = VOL_WIDTH // 2
    pooled_planes = depth_cells // 2
    grad_scale = 1.0 / math.sqrt(
        total_samples * depth_cells * space_count * VOL_HEIGHT * VOL_WIDTH / 8.0
    )
    kernel_one = kernel_of(first_weight, CH_IN)
    kernel_two = kernel_of(second_weight, CH_MID)
    haloed_in = padded_2(volumes, (("space", 2),), 1)
    padded_in = pad_sides(
        haloed_in.reshape(sample_count, CH_IN, depth_cells + 2, VOL_HEIGHT, VOL_WIDTH), 0, 1
    )
    first_pre = correlate(padded_in, kernel_one) + first_bias.reshape(1, CH_MID, 1, 1, 1)
    pooled = (
        jax.nn.silu(first_pre)
        .reshape(sample_count, CH_MID, pooled_planes, 2, half_height, 2, half_width, 2)
        .mean(axis=(3, 5, 7))
        .astype(jnp.bfloat16)
    )
    cot_cells = cotangent.reshape(sample_count, CH_OUT, pooled_planes, half_height, half_width)
    own_index = lax.axis_index("space")
    block_side = math.isqrt(space_count)
    bit_levels = block_side.bit_length() - 1
    pooled_block = slabs_to_blocks(
        pooled,
        lambda piece_in, bit_level: from_partner(piece_in, "space", bit_level),
        own_index,
        block_side,
        bit_levels,
    )
    cot_block = slabs_to_blocks(
        cot_cells,
        lambda piece_in, bit_level: from_partner(piece_in, "space", bit_level),
        own_index,
        block_side,
        bit_levels,
    )
    pooled_movers = (
        lambda piece_in: shifted(piece_in, "space", 1),
        lambda piece_in: shifted(piece_in, "space", -1),
        lambda piece_in: shifted(piece_in, "space", block_side),
        lambda piece_in: shifted(piece_in, "space", -block_side),
    )
    padded_pool = block_halo(pooled_block, pooled_movers, own_index, block_side)
    second_pre = correlate(padded_pool, kernel_two) + second_bias.reshape(1, CH_OUT, 1, 1, 1)
    second_grad = (cot_block.astype(jnp.float32) * silu_slope(second_pre)).astype(jnp.bfloat16)
    grad_movers = (
        lambda piece_in: shifted(piece_in, "space", 1),
        lambda piece_in: shifted(piece_in, "space", -1),
        lambda piece_in: shifted(piece_in, "space", block_side),
        lambda piece_in: shifted(piece_in, "space", -block_side),
    )
    padded_grad = block_halo(second_grad, grad_movers, own_index, block_side)
    grad_block = correlate(padded_grad, flipped(kernel_two))
    activation = blocks_to_slabs(
        jax.nn.silu(second_pre).astype(jnp.bfloat16),
        lambda piece_in, bit_level: from_partner(piece_in, "space", bit_level),
        own_index,
        block_side,
        bit_levels,
    )
    pooled_grad = blocks_to_slabs(
        grad_block,
        lambda piece_in, bit_level: from_partner(as_sent(piece_in), "space", bit_level).astype(
            piece_in.dtype
        ),
        own_index,
        block_side,
        bit_levels,
    )
    second_wgrad = weight_grad(padded_pool, second_grad)
    second_bgrad = jnp.sum(second_grad, axis=(0, 2, 3, 4), dtype=jnp.float32)
    pooled_cells = pooled_grad.reshape(sample_count, CH_MID, pooled_planes, half_height, half_width)
    first_grad = upsampled(pooled_cells, silu_slope(first_pre)).astype(jnp.bfloat16)
    first_wgrad = weight_grad(padded_in, first_grad)
    first_bgrad = jnp.sum(first_grad, axis=(0, 2, 3, 4), dtype=jnp.float32)
    first_wgrad, first_bgrad, second_wgrad, second_bgrad = all_summed(
        (first_wgrad, first_bgrad, second_wgrad, second_bgrad), ("space", "sample")
    )
    flip_one = flipped(kernel_one)
    haloed_grad = padded_2(
        first_grad.reshape(sample_count, CH_MID, depth_cells, plane_cells), (("space", 2),), 1
    )
    input_sum = correlate(
        pad_sides(
            haloed_grad.reshape(sample_count, CH_MID, depth_cells + 2, VOL_HEIGHT, VOL_WIDTH), 0, 1
        ),
        flip_one,
    )
    input_sum = input_sum.reshape(sample_count, CH_IN, depth_cells, plane_cells)
    input_grad = input_sum.astype(jnp.bfloat16)
    return (
        activation,
        input_grad,
        first_wgrad * grad_scale,
        first_bgrad * grad_scale,
        second_wgrad * grad_scale,
        second_bgrad * grad_scale,
    )


def solution(mesh):
    in_specs = (
        P("sample", None, "space", None),
        P(),
        P(),
        P(),
        P(),
        P("sample", None, "space", None),
    )
    out_specs = (
        P("sample", None, "space", None),
        P("sample", None, "space", None),
        P(),
        P(),
        P(),
        P(),
    )
    return jax.shard_map(
        per_device, mesh=mesh, in_specs=in_specs, out_specs=out_specs, check_vma=False
    )
```

```python
import math

import jax
import jax.numpy as jnp
from jax import lax
from jax.sharding import PartitionSpec as P

CH_IN = 32
CH_MID = 64
CH_OUT = 128
VOL_HEIGHT = 64
VOL_WIDTH = 16


LAYOUT_SPEC = ("NCDHW", "OIDHW", "NCDHW")


def padded_2(x, sides, width):
    for axis, dim in sides:
        size, length = (lax.axis_size(axis), x.shape[dim])
        up = [(i, (i + 1) % size) for i in range(size - 1)]
        down = [(j, i) for i, j in up]
        last = lax.slice_in_dim(x, length - width, length, axis=dim)
        initial = lax.slice_in_dim(x, 0, width, axis=dim)
        before = lax.ppermute(last, axis, up)
        after = lax.ppermute(initial, axis, down)
        x = jnp.concatenate([before, x, after], axis=dim)
    return x


def from_partner(block, axis, stride):
    count = lax.axis_size(axis)
    route = []
    for low in range(count):
        high = low | 1 << stride
        if high != low and high < count:
            route += [(low, high), (high, low)]
    return lax.ppermute(block, axis, route)


def shifted(x, axis, by):
    size = lax.axis_size(axis)
    pairs = [(i, i + by) for i in range(size) if 0 <= i + by < size]
    return lax.ppermute(x, axis, pairs)


def as_sent(x):

    def short(part):
        return part.astype(jnp.bfloat16) if part.dtype == jnp.float32 else part

    return jax.tree.map(short, x)


def kernel_of(weight, channels):
    return weight.reshape(weight.shape[0], 3, 3, 3, channels).transpose(0, 4, 1, 2, 3)


def flipped(kernel):
    return jnp.flip(kernel, (2, 3, 4)).transpose(1, 0, 2, 3, 4)


def correlate(padded, kernel):
    return lax.conv_general_dilated(
        padded,
        kernel,
        (1, 1, 1),
        "VALID",
        dimension_numbers=LAYOUT_SPEC,
        preferred_element_type=jnp.float32,
    )


def pad_sides(volume, depth_pad, height_pad):
    return jnp.pad(
        volume, ((0, 0), (0, 0), (depth_pad, depth_pad), (height_pad, height_pad), (1, 1))
    )


def silu_slope(values_in):
    sigmoid_v = jax.nn.sigmoid(values_in)
    return sigmoid_v * (1.0 + values_in * (1.0 - sigmoid_v))


def upsampled(pooled_grad, slope):
    sample_count, channels, planes, rows_half, cols_half = pooled_grad.shape
    shaped = slope.reshape(sample_count, channels, planes, 2, rows_half, 2, cols_half, 2)
    return (pooled_grad[:, :, :, None, :, None, :, None] * 0.125 * shaped).reshape(slope.shape)


def weight_grad(padded, slope_grad):
    summed = lax.conv_general_dilated(
        padded,
        slope_grad,
        (1, 1, 1),
        "VALID",
        dimension_numbers=("CNDHW", "IODHW", "CNDHW"),
        preferred_element_type=jnp.float32,
    )
    out_channels, in_channels = summed.shape[:2]
    return summed.transpose(0, 2, 3, 4, 1).reshape(out_channels, 27 * in_channels)


def butterfly(pieces_all, mover, own_index, bit_levels):
    for bit_level in range(bit_levels):
        step_size = 1 << bit_level
        outer_count = pieces_all.shape[0] // (2 * step_size)
        trailing = pieces_all.shape[1:]
        grouped = pieces_all.reshape((outer_count, 2, step_size) + trailing)
        lower_half = grouped[:, 0]
        upper_half = grouped[:, 1]
        bit_set = own_index >> bit_level & 1 == 1
        kept_half = jnp.where(bit_set, upper_half, lower_half)
        sent_half = jnp.where(bit_set, lower_half, upper_half)
        arrived = mover(sent_half, bit_level)
        new_lower = jnp.where(bit_set, arrived, kept_half)
        new_upper = jnp.where(bit_set, kept_half, arrived)
        pieces_all = jnp.stack([new_lower, new_upper], axis=1).reshape(pieces_all.shape)
    return pieces_all


def slabs_to_blocks(slab, mover, own_index, block_side, bit_levels):
    sample_count, channels, planes, rows_all, row_cells = slab.shape
    rows_block = rows_all // block_side
    pieces_all = jnp.moveaxis(
        slab.reshape(sample_count, channels, planes, block_side, rows_block * row_cells), 3, 0
    )
    arrived = jnp.moveaxis(butterfly(pieces_all, mover, own_index, bit_levels), 0, 2)
    return arrived.reshape(sample_count, channels, block_side * planes, rows_block, row_cells)


def blocks_to_slabs(block, mover, own_index, block_side, bit_levels):
    sample_count, channels, planes_all, rows_block, row_cells = block.shape
    planes = planes_all // block_side
    pieces_all = jnp.moveaxis(
        block.reshape(sample_count, channels, block_side, planes, rows_block * row_cells), 2, 0
    )
    arrived = jnp.moveaxis(butterfly(pieces_all, mover, own_index, bit_levels), 0, 3)
    return arrived.reshape(sample_count, channels, planes, block_side * rows_block * row_cells)


def block_halo(block, movers, own_index, block_side):
    sample_count, channels, planes, rows_block, row_cells = block.shape
    block_column = own_index % block_side
    last_row = block[:, :, :, rows_block - 1].reshape(sample_count, channels, planes * row_cells)
    first_row = block[:, :, :, 0].reshape(sample_count, channels, planes * row_cells)
    last_row = jnp.where(block_column == block_side - 1, jnp.zeros_like(last_row), last_row)
    first_row = jnp.where(block_column == 0, jnp.zeros_like(first_row), first_row)
    from_prev = movers[0](last_row)
    from_next = movers[1](first_row)
    tall_block = jnp.concatenate(
        [
            from_prev.reshape(sample_count, channels, planes, 1, row_cells),
            block,
            from_next.reshape(sample_count, channels, planes, 1, row_cells),
        ],
        axis=3,
    )
    top_plane = tall_block[:, :, planes - 1].reshape(
        sample_count, channels, (rows_block + 2) * row_cells
    )
    bottom_plane = tall_block[:, :, 0].reshape(sample_count, channels, (rows_block + 2) * row_cells)
    from_below = movers[2](top_plane)
    from_above = movers[3](bottom_plane)
    full_block = jnp.concatenate(
        [
            from_below.reshape(sample_count, channels, 1, rows_block + 2, row_cells),
            tall_block,
            from_above.reshape(sample_count, channels, 1, rows_block + 2, row_cells),
        ],
        axis=2,
    )
    return jnp.pad(full_block, ((0, 0), (0, 0), (0, 0), (0, 0), (1, 1)))


def all_summed(parts, axes):
    flat = jnp.concatenate([part.reshape(-1) for part in parts])
    levels = []
    for axis in axes:
        for bit in range(lax.axis_size(axis).bit_length() - 1):
            levels.append((axis, bit))
    block = 1 << len(levels)
    total = flat.shape[0]
    current = jnp.pad(flat, (0, -total % block))
    for axis, bit in levels:
        half = current.shape[0] // 2
        upper = (lax.axis_index(axis) >> bit & 1) == 1
        kept = jnp.where(upper, current[half:], current[:half])
        sent = jnp.where(upper, current[:half], current[half:])
        pairs = [(i, i ^ 1 << bit) for i in range(lax.axis_size(axis))]
        current = kept + lax.ppermute(sent, axis, pairs)
    for axis, bit in reversed(levels):
        upper = (lax.axis_index(axis) >> bit & 1) == 1
        pairs = [(i, i ^ 1 << bit) for i in range(lax.axis_size(axis))]
        other = lax.ppermute(current, axis, pairs)
        current = jnp.where(
            upper, jnp.concatenate([other, current]), jnp.concatenate([current, other])
        )
    results, start = [], 0
    for part in parts:
        results.append(current[start : start + part.size].reshape(part.shape))
        start += part.size
    return tuple(results)


def per_device(volumes, first_weight, first_bias, second_weight, second_bias, cotangent):
    sample_count = volumes.shape[0]
    depth_cells = volumes.shape[2]
    plane_cells = volumes.shape[3]
    space_count = lax.axis_size("space")
    total_samples = sample_count * lax.axis_size("sample")
    half_height = VOL_HEIGHT // 2
    half_width = VOL_WIDTH // 2
    pooled_planes = depth_cells // 2
    grad_scale = 1.0 / math.sqrt(
        total_samples * depth_cells * space_count * VOL_HEIGHT * VOL_WIDTH / 8.0
    )
    kernel_one = kernel_of(first_weight, CH_IN)
    kernel_two = kernel_of(second_weight, CH_MID)
    haloed_in = padded_2(volumes, (("space", 2),), 1)
    padded_in = pad_sides(
        haloed_in.reshape(sample_count, CH_IN, depth_cells + 2, VOL_HEIGHT, VOL_WIDTH), 0, 1
    )
    first_pre = correlate(padded_in, kernel_one) + first_bias.reshape(1, CH_MID, 1, 1, 1)
    pooled = (
        jax.nn.silu(first_pre)
        .reshape(sample_count, CH_MID, pooled_planes, 2, half_height, 2, half_width, 2)
        .mean(axis=(3, 5, 7))
        .astype(jnp.bfloat16)
    )
    cot_cells = cotangent.reshape(sample_count, CH_OUT, pooled_planes, half_height, half_width)
    pooled_cells_count = half_height * half_width
    haloed_pool = padded_2(
        pooled.reshape(sample_count, CH_MID, pooled_planes, pooled_cells_count), (("space", 2),), 1
    )
    padded_pool = pad_sides(
        haloed_pool.reshape(sample_count, CH_MID, pooled_planes + 2, half_height, half_width), 0, 1
    )
    second_pre = correlate(padded_pool, kernel_two) + second_bias.reshape(1, CH_OUT, 1, 1, 1)
    second_grad = (cot_cells.astype(jnp.float32) * silu_slope(second_pre)).astype(jnp.bfloat16)
    haloed_second = padded_2(
        second_grad.reshape(sample_count, CH_OUT, pooled_planes, pooled_cells_count),
        (("space", 2),),
        1,
    )
    padded_grad = pad_sides(
        haloed_second.reshape(sample_count, CH_OUT, pooled_planes + 2, half_height, half_width),
        0,
        1,
    )
    pooled_grad = correlate(padded_grad, flipped(kernel_two))
    activation = (
        jax.nn.silu(second_pre)
        .astype(jnp.bfloat16)
        .reshape(sample_count, CH_OUT, pooled_planes, pooled_cells_count)
    )
    second_wgrad = weight_grad(padded_pool, second_grad)
    second_bgrad = jnp.sum(second_grad, axis=(0, 2, 3, 4), dtype=jnp.float32)
    pooled_cells = pooled_grad
    first_grad = upsampled(pooled_cells, silu_slope(first_pre)).astype(jnp.bfloat16)
    first_wgrad = weight_grad(padded_in, first_grad)
    first_bgrad = jnp.sum(first_grad, axis=(0, 2, 3, 4), dtype=jnp.float32)
    first_wgrad, first_bgrad, second_wgrad, second_bgrad = all_summed(
        (first_wgrad, first_bgrad, second_wgrad, second_bgrad), ("space", "sample")
    )
    flip_one = flipped(kernel_one)
    haloed_grad = padded_2(
        first_grad.reshape(sample_count, CH_MID, depth_cells, plane_cells), (("space", 2),), 1
    )
    input_sum = correlate(
        pad_sides(
            haloed_grad.reshape(sample_count, CH_MID, depth_cells + 2, VOL_HEIGHT, VOL_WIDTH), 0, 1
        ),
        flip_one,
    )
    input_sum = input_sum.reshape(sample_count, CH_IN, depth_cells, plane_cells)
    input_grad = input_sum.astype(jnp.bfloat16)
    return (
        activation,
        input_grad,
        first_wgrad * grad_scale,
        first_bgrad * grad_scale,
        second_wgrad * grad_scale,
        second_bgrad * grad_scale,
    )


def solution(mesh):
    in_specs = (
        P("sample", None, "space", None),
        P(),
        P(),
        P(),
        P(),
        P("sample", None, "space", None),
    )
    out_specs = (
        P("sample", None, "space", None),
        P("sample", None, "space", None),
        P(),
        P(),
        P(),
        P(),
    )
    return jax.shard_map(
        per_device, mesh=mesh, in_specs=in_specs, out_specs=out_specs, check_vma=False
    )
```

```python
import math

import jax
import jax.numpy as jnp
from jax import lax
from jax.sharding import PartitionSpec as P

CH_IN = 32
CH_MID = 64
CH_OUT = 128
VOL_HEIGHT = 64
VOL_WIDTH = 16


LAYOUT_SPEC = ("NCDHW", "OIDHW", "NCDHW")


def padded_2(x, sides, width):
    for axis, dim in sides:
        size, length = (lax.axis_size(axis), x.shape[dim])
        up = [(i, (i + 1) % size) for i in range(size - 1)]
        down = [(j, i) for i, j in up]
        last = lax.slice_in_dim(x, length - width, length, axis=dim)
        initial = lax.slice_in_dim(x, 0, width, axis=dim)
        before = lax.ppermute(last, axis, up)
        after = lax.ppermute(initial, axis, down)
        x = jnp.concatenate([before, x, after], axis=dim)
    return x


def from_partner(block, axis, stride):
    count = lax.axis_size(axis)
    route = []
    for low in range(count):
        high = low | 1 << stride
        if high != low and high < count:
            route += [(low, high), (high, low)]
    return lax.ppermute(block, axis, route)


def shifted(x, axis, by):
    size = lax.axis_size(axis)
    pairs = [(i, i + by) for i in range(size) if 0 <= i + by < size]
    return lax.ppermute(x, axis, pairs)


def as_sent(x):

    def short(part):
        return part.astype(jnp.bfloat16) if part.dtype == jnp.float32 else part

    return jax.tree.map(short, x)


def kernel_of(weight, channels):
    return weight.reshape(weight.shape[0], 3, 3, 3, channels).transpose(0, 4, 1, 2, 3)


def flipped(kernel):
    return jnp.flip(kernel, (2, 3, 4)).transpose(1, 0, 2, 3, 4)


def correlate(padded, kernel):
    return lax.conv_general_dilated(
        padded,
        kernel,
        (1, 1, 1),
        "VALID",
        dimension_numbers=LAYOUT_SPEC,
        preferred_element_type=jnp.float32,
    )


def pad_sides(volume, depth_pad, height_pad):
    return jnp.pad(
        volume, ((0, 0), (0, 0), (depth_pad, depth_pad), (height_pad, height_pad), (1, 1))
    )


def silu_slope(values_in):
    sigmoid_v = jax.nn.sigmoid(values_in)
    return sigmoid_v * (1.0 + values_in * (1.0 - sigmoid_v))


def upsampled(pooled_grad, slope):
    sample_count, channels, planes, rows_half, cols_half = pooled_grad.shape
    shaped = slope.reshape(sample_count, channels, planes, 2, rows_half, 2, cols_half, 2)
    return (pooled_grad[:, :, :, None, :, None, :, None] * 0.125 * shaped).reshape(slope.shape)


def weight_grad(padded, slope_grad):
    depth_cells, height_cells, width_cells = slope_grad.shape[2:]
    windows = []
    for offset in range(27):
        depth_off, height_off, width_off = (offset // 9, offset // 3 % 3, offset % 3)
        windows.append(
            padded[
                :,
                :,
                depth_off : depth_off + depth_cells,
                height_off : height_off + height_cells,
                width_off : width_off + width_cells,
            ].reshape(padded.shape[0], padded.shape[1], -1)
        )
    patches = jnp.stack(windows, axis=1)
    summed = lax.dot_general(
        patches,
        slope_grad.reshape(slope_grad.shape[0], slope_grad.shape[1], -1),
        (((0, 3), (0, 2)), ((), ())),
        preferred_element_type=jnp.float32,
    )
    return summed.reshape(27 * padded.shape[1], slope_grad.shape[1])


def butterfly(pieces_all, mover, own_index, bit_levels):
    for bit_level in range(bit_levels):
        step_size = 1 << bit_level
        outer_count = pieces_all.shape[0] // (2 * step_size)
        trailing = pieces_all.shape[1:]
        grouped = pieces_all.reshape((outer_count, 2, step_size) + trailing)
        lower_half = grouped[:, 0]
        upper_half = grouped[:, 1]
        bit_set = own_index >> bit_level & 1 == 1
        kept_half = jnp.where(bit_set, upper_half, lower_half)
        sent_half = jnp.where(bit_set, lower_half, upper_half)
        arrived = mover(sent_half, bit_level)
        new_lower = jnp.where(bit_set, arrived, kept_half)
        new_upper = jnp.where(bit_set, kept_half, arrived)
        pieces_all = jnp.stack([new_lower, new_upper], axis=1).reshape(pieces_all.shape)
    return pieces_all


def slabs_to_blocks(slab, mover, own_index, block_side, bit_levels):
    sample_count, channels, planes, rows_all, row_cells = slab.shape
    rows_block = rows_all // block_side
    pieces_all = jnp.moveaxis(
        slab.reshape(sample_count, channels, planes, block_side, rows_block * row_cells), 3, 0
    )
    arrived = jnp.moveaxis(butterfly(pieces_all, mover, own_index, bit_levels), 0, 2)
    return arrived.reshape(sample_count, channels, block_side * planes, rows_block, row_cells)


def blocks_to_slabs(block, mover, own_index, block_side, bit_levels):
    sample_count, channels, planes_all, rows_block, row_cells = block.shape
    planes = planes_all // block_side
    pieces_all = jnp.moveaxis(
        block.reshape(sample_count, channels, block_side, planes, rows_block * row_cells), 2, 0
    )
    arrived = jnp.moveaxis(butterfly(pieces_all, mover, own_index, bit_levels), 0, 3)
    return arrived.reshape(sample_count, channels, planes, block_side * rows_block * row_cells)


def block_halo(block, movers, own_index, block_side):
    sample_count, channels, planes, rows_block, row_cells = block.shape
    block_column = own_index % block_side
    last_row = block[:, :, :, rows_block - 1].reshape(sample_count, channels, planes * row_cells)
    first_row = block[:, :, :, 0].reshape(sample_count, channels, planes * row_cells)
    last_row = jnp.where(block_column == block_side - 1, jnp.zeros_like(last_row), last_row)
    first_row = jnp.where(block_column == 0, jnp.zeros_like(first_row), first_row)
    from_prev = movers[0](last_row)
    from_next = movers[1](first_row)
    tall_block = jnp.concatenate(
        [
            from_prev.reshape(sample_count, channels, planes, 1, row_cells),
            block,
            from_next.reshape(sample_count, channels, planes, 1, row_cells),
        ],
        axis=3,
    )
    top_plane = tall_block[:, :, planes - 1].reshape(
        sample_count, channels, (rows_block + 2) * row_cells
    )
    bottom_plane = tall_block[:, :, 0].reshape(sample_count, channels, (rows_block + 2) * row_cells)
    from_below = movers[2](top_plane)
    from_above = movers[3](bottom_plane)
    full_block = jnp.concatenate(
        [
            from_below.reshape(sample_count, channels, 1, rows_block + 2, row_cells),
            tall_block,
            from_above.reshape(sample_count, channels, 1, rows_block + 2, row_cells),
        ],
        axis=2,
    )
    return jnp.pad(full_block, ((0, 0), (0, 0), (0, 0), (0, 0), (1, 1)))


def all_summed(parts, axes):
    lanes = max(part.shape[-1] for part in parts)
    rows = [
        jnp.pad(part.reshape((-1, part.shape[-1])), ((0, 0), (0, lanes - part.shape[-1])))
        for part in parts
    ]
    stacked = jnp.concatenate(rows, axis=0)
    levels = []
    for axis in axes:
        for bit in range(lax.axis_size(axis).bit_length() - 1):
            levels.append((axis, bit))
    block = 8 << len(levels)
    total = stacked.shape[0]
    current = jnp.pad(stacked, ((0, -total % block), (0, 0)))
    for axis, bit in levels:
        half = current.shape[0] // 2
        upper = (lax.axis_index(axis) >> bit & 1) == 1
        kept = jnp.where(upper, current[half:], current[:half])
        sent = jnp.where(upper, current[:half], current[half:])
        pairs = [(i, i ^ 1 << bit) for i in range(lax.axis_size(axis))]
        current = kept + lax.ppermute(sent, axis, pairs)
    for axis, bit in reversed(levels):
        upper = (lax.axis_index(axis) >> bit & 1) == 1
        pairs = [(i, i ^ 1 << bit) for i in range(lax.axis_size(axis))]
        other = lax.ppermute(current, axis, pairs)
        current = jnp.where(
            upper, jnp.concatenate([other, current]), jnp.concatenate([current, other])
        )
    results, start = [], 0
    for part, row in zip(parts, rows):
        count = row.shape[0]
        piece = current[start : start + count, : part.shape[-1]]
        results.append(piece.reshape(part.shape))
        start += count
    return tuple(results)


def per_device(volumes, first_weight, first_bias, second_weight, second_bias, cotangent):
    sample_count = volumes.shape[0]
    depth_cells = volumes.shape[2]
    plane_cells = volumes.shape[3]
    space_count = lax.axis_size("space")
    total_samples = sample_count * lax.axis_size("sample")
    half_height = VOL_HEIGHT // 2
    half_width = VOL_WIDTH // 2
    pooled_planes = depth_cells // 2
    grad_scale = 1.0 / math.sqrt(
        total_samples * depth_cells * space_count * VOL_HEIGHT * VOL_WIDTH / 8.0
    )
    kernel_one = kernel_of(first_weight, CH_IN)
    kernel_two = kernel_of(second_weight, CH_MID)
    haloed_in = padded_2(volumes, (("space", 2),), 1)
    padded_in = pad_sides(
        haloed_in.reshape(sample_count, CH_IN, depth_cells + 2, VOL_HEIGHT, VOL_WIDTH), 0, 1
    )
    first_pre = correlate(padded_in, kernel_one) + first_bias.reshape(1, CH_MID, 1, 1, 1)
    pooled = (
        jax.nn.silu(first_pre)
        .reshape(sample_count, CH_MID, pooled_planes, 2, half_height, 2, half_width, 2)
        .mean(axis=(3, 5, 7))
        .astype(jnp.bfloat16)
    )
    cot_cells = cotangent.reshape(sample_count, CH_OUT, pooled_planes, half_height, half_width)
    pooled_cells_count = half_height * half_width
    haloed_pool = padded_2(
        pooled.reshape(sample_count, CH_MID, pooled_planes, pooled_cells_count), (("space", 2),), 1
    )
    padded_pool = pad_sides(
        haloed_pool.reshape(sample_count, CH_MID, pooled_planes + 2, half_height, half_width), 0, 1
    )
    second_pre = correlate(padded_pool, kernel_two) + second_bias.reshape(1, CH_OUT, 1, 1, 1)
    second_grad = (cot_cells.astype(jnp.float32) * silu_slope(second_pre)).astype(jnp.bfloat16)
    haloed_second = padded_2(
        second_grad.reshape(sample_count, CH_OUT, pooled_planes, pooled_cells_count),
        (("space", 2),),
        1,
    )
    padded_grad = pad_sides(
        haloed_second.reshape(sample_count, CH_OUT, pooled_planes + 2, half_height, half_width),
        0,
        1,
    )
    pooled_grad = correlate(padded_grad, flipped(kernel_two))
    activation = (
        jax.nn.silu(second_pre)
        .astype(jnp.bfloat16)
        .reshape(sample_count, CH_OUT, pooled_planes, pooled_cells_count)
    )
    second_wgrad = weight_grad(padded_pool, second_grad)
    second_bgrad = jnp.sum(second_grad, axis=(0, 2, 3, 4), dtype=jnp.float32)
    pooled_cells = pooled_grad
    first_grad = upsampled(pooled_cells, silu_slope(first_pre)).astype(jnp.bfloat16)
    first_wgrad = weight_grad(padded_in, first_grad)
    first_bgrad = jnp.sum(first_grad, axis=(0, 2, 3, 4), dtype=jnp.float32)
    first_wgrad, first_bgrad, second_wgrad, second_bgrad = all_summed(
        (first_wgrad, first_bgrad.reshape(1, -1), second_wgrad, second_bgrad.reshape(1, -1)),
        ("space", "sample"),
    )
    flip_one = flipped(kernel_one)
    haloed_grad = padded_2(
        first_grad.reshape(sample_count, CH_MID, depth_cells, plane_cells), (("space", 2),), 1
    )
    input_sum = correlate(
        pad_sides(
            haloed_grad.reshape(sample_count, CH_MID, depth_cells + 2, VOL_HEIGHT, VOL_WIDTH), 0, 1
        ),
        flip_one,
    )
    input_sum = input_sum.reshape(sample_count, CH_IN, depth_cells, plane_cells)
    input_grad = input_sum.astype(jnp.bfloat16)
    return (
        activation,
        input_grad,
        first_wgrad.T * grad_scale,
        first_bgrad.reshape(-1) * grad_scale,
        second_wgrad.T * grad_scale,
        second_bgrad.reshape(-1) * grad_scale,
    )


def solution(mesh):
    in_specs = (
        P("sample", None, "space", None),
        P(),
        P(),
        P(),
        P(),
        P("sample", None, "space", None),
    )
    out_specs = (
        P("sample", None, "space", None),
        P("sample", None, "space", None),
        P(),
        P(),
        P(),
        P(),
    )
    return jax.shard_map(
        per_device, mesh=mesh, in_specs=in_specs, out_specs=out_specs, check_vma=False
    )
```

```python
import math

import jax
import jax.numpy as jnp
from jax import lax
from jax.sharding import PartitionSpec as P

CH_IN = 32
CH_MID = 64
CH_OUT = 128
VOL_HEIGHT = 64
VOL_WIDTH = 16


LAYOUT_SPEC = ("NCDHW", "OIDHW", "NCDHW")


def padded_2(x, sides, width):
    for axis, dim in sides:
        size, length = (lax.axis_size(axis), x.shape[dim])
        up = [(i, (i + 1) % size) for i in range(size - 1)]
        down = [(j, i) for i, j in up]
        last = lax.slice_in_dim(x, length - width, length, axis=dim)
        initial = lax.slice_in_dim(x, 0, width, axis=dim)
        before = lax.ppermute(last, axis, up)
        after = lax.ppermute(initial, axis, down)
        x = jnp.concatenate([before, x, after], axis=dim)
    return x


def from_partner(block, axis, stride):
    count = lax.axis_size(axis)
    route = []
    for low in range(count):
        high = low | 1 << stride
        if high != low and high < count:
            route += [(low, high), (high, low)]
    return lax.ppermute(block, axis, route)


def shifted(x, axis, by):
    size = lax.axis_size(axis)
    pairs = [(i, i + by) for i in range(size) if 0 <= i + by < size]
    return lax.ppermute(x, axis, pairs)


def as_sent(x):

    def short(part):
        return part.astype(jnp.bfloat16) if part.dtype == jnp.float32 else part

    return jax.tree.map(short, x)


def kernel_of(weight, channels):
    return weight.reshape(weight.shape[0], 3, 3, 3, channels).transpose(0, 4, 1, 2, 3)


def flipped(kernel):
    return jnp.flip(kernel, (2, 3, 4)).transpose(1, 0, 2, 3, 4)


def correlate(padded, kernel):
    return lax.conv_general_dilated(
        padded,
        kernel,
        (1, 1, 1),
        "VALID",
        dimension_numbers=LAYOUT_SPEC,
        preferred_element_type=jnp.float32,
    )


def pad_sides(volume, depth_pad, height_pad):
    return jnp.pad(
        volume, ((0, 0), (0, 0), (depth_pad, depth_pad), (height_pad, height_pad), (1, 1))
    )


def silu_slope(values_in):
    sigmoid_v = jax.nn.sigmoid(values_in)
    return sigmoid_v * (1.0 + values_in * (1.0 - sigmoid_v))


def upsampled(pooled_grad, slope):
    sample_count, channels, planes, rows_half, cols_half = pooled_grad.shape
    shaped = slope.reshape(sample_count, channels, planes, 2, rows_half, 2, cols_half, 2)
    return (pooled_grad[:, :, :, None, :, None, :, None] * 0.125 * shaped).reshape(slope.shape)


def weight_grad(padded, slope_grad):
    summed = lax.conv_general_dilated(
        padded,
        slope_grad,
        (1, 1, 1),
        "VALID",
        dimension_numbers=("CNDHW", "IODHW", "CNDHW"),
        preferred_element_type=jnp.float32,
    )
    out_channels, in_channels = summed.shape[:2]
    return summed.transpose(0, 2, 3, 4, 1).reshape(out_channels, 27 * in_channels)


def weight_grad_by_offset(padded, slope_grad):
    depth_cells, height_cells, width_cells = slope_grad.shape[2:]
    columns = []
    for offset in range(27):
        depth_off, height_off, width_off = (offset // 9, offset // 3 % 3, offset % 3)
        window = padded[
            :,
            :,
            depth_off : depth_off + depth_cells,
            height_off : height_off + height_cells,
            width_off : width_off + width_cells,
        ]
        columns.append(
            lax.dot_general(
                window,
                slope_grad,
                (((0, 2, 3, 4), (0, 2, 3, 4)), ((), ())),
                preferred_element_type=jnp.float32,
            )
        )
    return jnp.stack(columns).reshape(27 * padded.shape[1], slope_grad.shape[1]).T


def butterfly(pieces_all, mover, own_index, bit_levels):
    for bit_level in range(bit_levels):
        step_size = 1 << bit_level
        outer_count = pieces_all.shape[0] // (2 * step_size)
        trailing = pieces_all.shape[1:]
        grouped = pieces_all.reshape((outer_count, 2, step_size) + trailing)
        lower_half = grouped[:, 0]
        upper_half = grouped[:, 1]
        bit_set = own_index >> bit_level & 1 == 1
        kept_half = jnp.where(bit_set, upper_half, lower_half)
        sent_half = jnp.where(bit_set, lower_half, upper_half)
        arrived = mover(sent_half, bit_level)
        new_lower = jnp.where(bit_set, arrived, kept_half)
        new_upper = jnp.where(bit_set, kept_half, arrived)
        pieces_all = jnp.stack([new_lower, new_upper], axis=1).reshape(pieces_all.shape)
    return pieces_all


def slabs_to_blocks(slab, mover, own_index, block_side, bit_levels):
    sample_count, channels, planes, rows_all, row_cells = slab.shape
    rows_block = rows_all // block_side
    pieces_all = jnp.moveaxis(
        slab.reshape(sample_count, channels, planes, block_side, rows_block * row_cells), 3, 0
    )
    arrived = jnp.moveaxis(butterfly(pieces_all, mover, own_index, bit_levels), 0, 2)
    return arrived.reshape(sample_count, channels, block_side * planes, rows_block, row_cells)


def blocks_to_slabs(block, mover, own_index, block_side, bit_levels):
    sample_count, channels, planes_all, rows_block, row_cells = block.shape
    planes = planes_all // block_side
    pieces_all = jnp.moveaxis(
        block.reshape(sample_count, channels, block_side, planes, rows_block * row_cells), 2, 0
    )
    arrived = jnp.moveaxis(butterfly(pieces_all, mover, own_index, bit_levels), 0, 3)
    return arrived.reshape(sample_count, channels, planes, block_side * rows_block * row_cells)


def block_halo(block, movers, own_index, block_side):
    sample_count, channels, planes, rows_block, row_cells = block.shape
    block_column = own_index % block_side
    last_row = block[:, :, :, rows_block - 1].reshape(sample_count, channels, planes * row_cells)
    first_row = block[:, :, :, 0].reshape(sample_count, channels, planes * row_cells)
    last_row = jnp.where(block_column == block_side - 1, jnp.zeros_like(last_row), last_row)
    first_row = jnp.where(block_column == 0, jnp.zeros_like(first_row), first_row)
    from_prev = movers[0](last_row)
    from_next = movers[1](first_row)
    tall_block = jnp.concatenate(
        [
            from_prev.reshape(sample_count, channels, planes, 1, row_cells),
            block,
            from_next.reshape(sample_count, channels, planes, 1, row_cells),
        ],
        axis=3,
    )
    top_plane = tall_block[:, :, planes - 1].reshape(
        sample_count, channels, (rows_block + 2) * row_cells
    )
    bottom_plane = tall_block[:, :, 0].reshape(sample_count, channels, (rows_block + 2) * row_cells)
    from_below = movers[2](top_plane)
    from_above = movers[3](bottom_plane)
    full_block = jnp.concatenate(
        [
            from_below.reshape(sample_count, channels, 1, rows_block + 2, row_cells),
            tall_block,
            from_above.reshape(sample_count, channels, 1, rows_block + 2, row_cells),
        ],
        axis=2,
    )
    return jnp.pad(full_block, ((0, 0), (0, 0), (0, 0), (0, 0), (1, 1)))


def all_summed(parts, axes):
    flat = jnp.concatenate([part.reshape(-1) for part in parts])
    levels = []
    for axis in axes:
        for bit in range(lax.axis_size(axis).bit_length() - 1):
            levels.append((axis, bit))
    block = 1 << len(levels)
    total = flat.shape[0]
    current = jnp.pad(flat, (0, -total % block))
    for axis, bit in levels:
        half = current.shape[0] // 2
        upper = (lax.axis_index(axis) >> bit & 1) == 1
        kept = jnp.where(upper, current[half:], current[:half])
        sent = jnp.where(upper, current[:half], current[half:])
        pairs = [(i, i ^ 1 << bit) for i in range(lax.axis_size(axis))]
        current = kept + lax.ppermute(sent, axis, pairs)
    for axis, bit in reversed(levels):
        upper = (lax.axis_index(axis) >> bit & 1) == 1
        pairs = [(i, i ^ 1 << bit) for i in range(lax.axis_size(axis))]
        other = lax.ppermute(current, axis, pairs)
        current = jnp.where(
            upper, jnp.concatenate([other, current]), jnp.concatenate([current, other])
        )
    results, start = [], 0
    for part in parts:
        results.append(current[start : start + part.size].reshape(part.shape))
        start += part.size
    return tuple(results)


def per_device(volumes, first_weight, first_bias, second_weight, second_bias, cotangent):
    sample_count = volumes.shape[0]
    depth_cells = volumes.shape[2]
    plane_cells = volumes.shape[3]
    space_count = lax.axis_size("space")
    total_samples = sample_count * lax.axis_size("sample")
    half_height = VOL_HEIGHT // 2
    half_width = VOL_WIDTH // 2
    pooled_planes = depth_cells // 2
    grad_scale = 1.0 / math.sqrt(
        total_samples * depth_cells * space_count * VOL_HEIGHT * VOL_WIDTH / 8.0
    )
    kernel_one = kernel_of(first_weight, CH_IN)
    kernel_two = kernel_of(second_weight, CH_MID)
    haloed_in = padded_2(volumes, (("space", 2),), 1)
    padded_in = pad_sides(
        haloed_in.reshape(sample_count, CH_IN, depth_cells + 2, VOL_HEIGHT, VOL_WIDTH), 0, 1
    )
    first_pre = correlate(padded_in, kernel_one) + first_bias.reshape(1, CH_MID, 1, 1, 1)
    pooled = (
        jax.nn.silu(first_pre)
        .reshape(sample_count, CH_MID, pooled_planes, 2, half_height, 2, half_width, 2)
        .mean(axis=(3, 5, 7))
        .astype(jnp.bfloat16)
    )
    cot_cells = cotangent.reshape(sample_count, CH_OUT, pooled_planes, half_height, half_width)
    pooled_cells_count = half_height * half_width
    haloed_pool = padded_2(
        pooled.reshape(sample_count, CH_MID, pooled_planes, pooled_cells_count), (("space", 2),), 1
    )
    padded_pool = pad_sides(
        haloed_pool.reshape(sample_count, CH_MID, pooled_planes + 2, half_height, half_width), 0, 1
    )
    second_pre = correlate(padded_pool, kernel_two) + second_bias.reshape(1, CH_OUT, 1, 1, 1)
    second_grad = (cot_cells.astype(jnp.float32) * silu_slope(second_pre)).astype(jnp.bfloat16)
    haloed_second = padded_2(
        second_grad.reshape(sample_count, CH_OUT, pooled_planes, pooled_cells_count),
        (("space", 2),),
        1,
    )
    padded_grad = pad_sides(
        haloed_second.reshape(sample_count, CH_OUT, pooled_planes + 2, half_height, half_width),
        0,
        1,
    )
    pooled_grad = correlate(padded_grad, flipped(kernel_two))
    activation = (
        jax.nn.silu(second_pre)
        .astype(jnp.bfloat16)
        .reshape(sample_count, CH_OUT, pooled_planes, pooled_cells_count)
    )
    second_wgrad = weight_grad(padded_pool, second_grad)
    second_bgrad = jnp.sum(second_grad, axis=(0, 2, 3, 4), dtype=jnp.float32)
    pooled_cells = pooled_grad
    first_grad = upsampled(pooled_cells, silu_slope(first_pre)).astype(jnp.bfloat16)
    first_wgrad = weight_grad_by_offset(padded_in, first_grad)
    first_bgrad = jnp.sum(first_grad, axis=(0, 2, 3, 4), dtype=jnp.float32)
    first_wgrad, first_bgrad, second_wgrad, second_bgrad = all_summed(
        (first_wgrad, first_bgrad, second_wgrad, second_bgrad), ("space", "sample")
    )
    flip_one = flipped(kernel_one)
    haloed_grad = padded_2(
        first_grad.reshape(sample_count, CH_MID, depth_cells, plane_cells), (("space", 2),), 1
    )
    input_sum = correlate(
        pad_sides(
            haloed_grad.reshape(sample_count, CH_MID, depth_cells + 2, VOL_HEIGHT, VOL_WIDTH), 0, 1
        ),
        flip_one,
    )
    input_sum = input_sum.reshape(sample_count, CH_IN, depth_cells, plane_cells)
    input_grad = input_sum.astype(jnp.bfloat16)
    return (
        activation,
        input_grad,
        first_wgrad * grad_scale,
        first_bgrad * grad_scale,
        second_wgrad * grad_scale,
        second_bgrad * grad_scale,
    )


def solution(mesh):
    in_specs = (
        P("sample", None, "space", None),
        P(),
        P(),
        P(),
        P(),
        P("sample", None, "space", None),
    )
    out_specs = (
        P("sample", None, "space", None),
        P("sample", None, "space", None),
        P(),
        P(),
        P(),
        P(),
    )
    return jax.shard_map(
        per_device, mesh=mesh, in_specs=in_specs, out_specs=out_specs, check_vma=False
    )
```

```python
import math

import jax
import jax.numpy as jnp
from jax import lax
from jax.sharding import PartitionSpec as P

CH_IN = 32
CH_MID = 64
CH_OUT = 128
VOL_HEIGHT = 64
VOL_WIDTH = 16


LAYOUT_SPEC = ("NCDHW", "OIDHW", "NCDHW")


def padded_2(x, sides, width):
    for axis, dim in sides:
        size, length = (lax.axis_size(axis), x.shape[dim])
        up = [(i, (i + 1) % size) for i in range(size - 1)]
        down = [(j, i) for i, j in up]
        last = lax.slice_in_dim(x, length - width, length, axis=dim)
        initial = lax.slice_in_dim(x, 0, width, axis=dim)
        before = lax.ppermute(last, axis, up)
        after = lax.ppermute(initial, axis, down)
        x = jnp.concatenate([before, x, after], axis=dim)
    return x


def from_partner(block, axis, stride):
    count = lax.axis_size(axis)
    route = []
    for low in range(count):
        high = low | 1 << stride
        if high != low and high < count:
            route += [(low, high), (high, low)]
    return lax.ppermute(block, axis, route)


def shifted(x, axis, by):
    size = lax.axis_size(axis)
    pairs = [(i, i + by) for i in range(size) if 0 <= i + by < size]
    return lax.ppermute(x, axis, pairs)


def as_sent(x):

    def short(part):
        return part.astype(jnp.bfloat16) if part.dtype == jnp.float32 else part

    return jax.tree.map(short, x)


def kernel_of(weight, channels):
    return weight.reshape(weight.shape[0], 3, 3, 3, channels).transpose(0, 4, 1, 2, 3)


def flipped(kernel):
    return jnp.flip(kernel, (2, 3, 4)).transpose(1, 0, 2, 3, 4)


def correlate(padded, kernel):
    return lax.conv_general_dilated(
        padded,
        kernel,
        (1, 1, 1),
        "VALID",
        dimension_numbers=LAYOUT_SPEC,
        preferred_element_type=jnp.float32,
    )


def pad_sides(volume, depth_pad, height_pad):
    return jnp.pad(
        volume, ((0, 0), (0, 0), (depth_pad, depth_pad), (height_pad, height_pad), (1, 1))
    )


def silu_slope(values_in):
    sigmoid_v = jax.nn.sigmoid(values_in)
    return sigmoid_v * (1.0 + values_in * (1.0 - sigmoid_v))


def upsampled(pooled_grad, slope):
    sample_count, channels, planes, rows_half, cols_half = pooled_grad.shape
    shaped = slope.reshape(sample_count, channels, planes, 2, rows_half, 2, cols_half, 2)
    return (pooled_grad[:, :, :, None, :, None, :, None] * 0.125 * shaped).reshape(slope.shape)


def weight_grad(padded, slope_grad):
    summed = lax.conv_general_dilated(
        padded,
        slope_grad,
        (1, 1, 1),
        "VALID",
        dimension_numbers=("CNDHW", "IODHW", "CNDHW"),
        preferred_element_type=jnp.float32,
    )
    out_channels, in_channels = summed.shape[:2]
    return summed.transpose(0, 2, 3, 4, 1).reshape(out_channels, 27 * in_channels)


def butterfly(pieces_all, mover, own_index, bit_levels):
    for bit_level in range(bit_levels):
        step_size = 1 << bit_level
        outer_count = pieces_all.shape[0] // (2 * step_size)
        trailing = pieces_all.shape[1:]
        grouped = pieces_all.reshape((outer_count, 2, step_size) + trailing)
        lower_half = grouped[:, 0]
        upper_half = grouped[:, 1]
        bit_set = own_index >> bit_level & 1 == 1
        kept_half = jnp.where(bit_set, upper_half, lower_half)
        sent_half = jnp.where(bit_set, lower_half, upper_half)
        arrived = mover(sent_half, bit_level)
        new_lower = jnp.where(bit_set, arrived, kept_half)
        new_upper = jnp.where(bit_set, kept_half, arrived)
        pieces_all = jnp.stack([new_lower, new_upper], axis=1).reshape(pieces_all.shape)
    return pieces_all


def slabs_to_blocks(slab, mover, own_index, block_side, bit_levels):
    sample_count, channels, planes, rows_all, row_cells = slab.shape
    rows_block = rows_all // block_side
    pieces_all = jnp.moveaxis(
        slab.reshape(sample_count, channels, planes, block_side, rows_block * row_cells), 3, 0
    )
    arrived = jnp.moveaxis(butterfly(pieces_all, mover, own_index, bit_levels), 0, 2)
    return arrived.reshape(sample_count, channels, block_side * planes, rows_block, row_cells)


def blocks_to_slabs(block, mover, own_index, block_side, bit_levels):
    sample_count, channels, planes_all, rows_block, row_cells = block.shape
    planes = planes_all // block_side
    pieces_all = jnp.moveaxis(
        block.reshape(sample_count, channels, block_side, planes, rows_block * row_cells), 2, 0
    )
    arrived = jnp.moveaxis(butterfly(pieces_all, mover, own_index, bit_levels), 0, 3)
    return arrived.reshape(sample_count, channels, planes, block_side * rows_block * row_cells)


def block_halo(block, movers, own_index, block_side):
    sample_count, channels, planes, rows_block, row_cells = block.shape
    block_column = own_index % block_side
    last_row = block[:, :, :, rows_block - 1].reshape(sample_count, channels, planes * row_cells)
    first_row = block[:, :, :, 0].reshape(sample_count, channels, planes * row_cells)
    last_row = jnp.where(block_column == block_side - 1, jnp.zeros_like(last_row), last_row)
    first_row = jnp.where(block_column == 0, jnp.zeros_like(first_row), first_row)
    from_prev = movers[0](last_row)
    from_next = movers[1](first_row)
    tall_block = jnp.concatenate(
        [
            from_prev.reshape(sample_count, channels, planes, 1, row_cells),
            block,
            from_next.reshape(sample_count, channels, planes, 1, row_cells),
        ],
        axis=3,
    )
    top_plane = tall_block[:, :, planes - 1].reshape(
        sample_count, channels, (rows_block + 2) * row_cells
    )
    bottom_plane = tall_block[:, :, 0].reshape(sample_count, channels, (rows_block + 2) * row_cells)
    from_below = movers[2](top_plane)
    from_above = movers[3](bottom_plane)
    full_block = jnp.concatenate(
        [
            from_below.reshape(sample_count, channels, 1, rows_block + 2, row_cells),
            tall_block,
            from_above.reshape(sample_count, channels, 1, rows_block + 2, row_cells),
        ],
        axis=2,
    )
    return jnp.pad(full_block, ((0, 0), (0, 0), (0, 0), (0, 0), (1, 1)))


def all_summed(parts, axes):
    flat = jnp.concatenate([part.reshape(-1) for part in parts])
    levels = []
    for axis in axes:
        for bit in range(lax.axis_size(axis).bit_length() - 1):
            levels.append((axis, bit))
    block = 1 << len(levels)
    total = flat.shape[0]
    current = jnp.pad(flat, (0, -total % block))
    for axis, bit in levels:
        half = current.shape[0] // 2
        upper = (lax.axis_index(axis) >> bit & 1) == 1
        kept = jnp.where(upper, current[half:], current[:half])
        sent = jnp.where(upper, current[:half], current[half:])
        pairs = [(i, i ^ 1 << bit) for i in range(lax.axis_size(axis))]
        current = kept + lax.ppermute(sent, axis, pairs)
    for axis, bit in reversed(levels):
        upper = (lax.axis_index(axis) >> bit & 1) == 1
        pairs = [(i, i ^ 1 << bit) for i in range(lax.axis_size(axis))]
        other = lax.ppermute(current, axis, pairs)
        current = jnp.where(
            upper, jnp.concatenate([other, current]), jnp.concatenate([current, other])
        )
    results, start = [], 0
    for part in parts:
        results.append(current[start : start + part.size].reshape(part.shape))
        start += part.size
    return tuple(results)


def per_device(volumes, first_weight, first_bias, second_weight, second_bias, cotangent):
    sample_count = volumes.shape[0]
    depth_cells = volumes.shape[2]
    plane_cells = volumes.shape[3]
    space_count = lax.axis_size("space")
    total_samples = sample_count * lax.axis_size("sample")
    half_height = VOL_HEIGHT // 2
    half_width = VOL_WIDTH // 2
    pooled_planes = depth_cells // 2
    grad_scale = 1.0 / math.sqrt(
        total_samples * depth_cells * space_count * VOL_HEIGHT * VOL_WIDTH / 8.0
    )
    kernel_one = kernel_of(first_weight, CH_IN)
    kernel_two = kernel_of(second_weight, CH_MID)
    haloed_in = padded_2(volumes, (("space", 2),), 1)
    padded_in = pad_sides(
        haloed_in.reshape(sample_count, CH_IN, depth_cells + 2, VOL_HEIGHT, VOL_WIDTH), 0, 1
    )
    first_pre = correlate(padded_in, kernel_one) + first_bias.reshape(1, CH_MID, 1, 1, 1)
    pooled = (
        jax.nn.silu(first_pre)
        .reshape(sample_count, CH_MID, pooled_planes, 2, half_height, 2, half_width, 2)
        .mean(axis=(3, 5, 7))
        .astype(jnp.bfloat16)
    )
    cot_cells = cotangent.reshape(sample_count, CH_OUT, pooled_planes, half_height, half_width)
    pooled_cells_count = half_height * half_width
    haloed_pool = padded_2(
        pooled.reshape(sample_count, CH_MID, pooled_planes, pooled_cells_count), (("space", 2),), 1
    )
    padded_pool = pad_sides(
        haloed_pool.reshape(sample_count, CH_MID, pooled_planes + 2, half_height, half_width), 0, 1
    )
    second_pre = correlate(padded_pool, kernel_two) + second_bias.reshape(1, CH_OUT, 1, 1, 1)
    second_grad = (cot_cells.astype(jnp.float32) * silu_slope(second_pre)).astype(jnp.bfloat16)
    haloed_second = padded_2(
        second_grad.reshape(sample_count, CH_OUT, pooled_planes, pooled_cells_count),
        (("space", 2),),
        1,
    )
    padded_grad = pad_sides(
        haloed_second.reshape(sample_count, CH_OUT, pooled_planes + 2, half_height, half_width),
        0,
        1,
    )
    pooled_grad = correlate(padded_grad, flipped(kernel_two))
    activation = (
        jax.nn.silu(second_pre)
        .astype(jnp.bfloat16)
        .reshape(sample_count, CH_OUT, pooled_planes, pooled_cells_count)
    )
    second_wgrad = weight_grad(padded_pool, second_grad)
    second_bgrad = jnp.sum(second_grad, axis=(0, 2, 3, 4), dtype=jnp.float32)
    second_wgrad, second_bgrad = all_summed((second_wgrad, second_bgrad), ("space", "sample"))
    pooled_cells = pooled_grad
    first_grad = upsampled(pooled_cells, silu_slope(first_pre)).astype(jnp.bfloat16)
    first_wgrad = weight_grad(padded_in, first_grad)
    first_bgrad = jnp.sum(first_grad, axis=(0, 2, 3, 4), dtype=jnp.float32)
    first_wgrad, first_bgrad = all_summed((first_wgrad, first_bgrad), ("space", "sample"))
    flip_one = flipped(kernel_one)
    haloed_grad = padded_2(
        first_grad.reshape(sample_count, CH_MID, depth_cells, plane_cells), (("space", 2),), 1
    )
    input_sum = correlate(
        pad_sides(
            haloed_grad.reshape(sample_count, CH_MID, depth_cells + 2, VOL_HEIGHT, VOL_WIDTH), 0, 1
        ),
        flip_one,
    )
    input_sum = input_sum.reshape(sample_count, CH_IN, depth_cells, plane_cells)
    input_grad = input_sum.astype(jnp.bfloat16)
    return (
        activation,
        input_grad,
        first_wgrad * grad_scale,
        first_bgrad * grad_scale,
        second_wgrad * grad_scale,
        second_bgrad * grad_scale,
    )


def solution(mesh):
    in_specs = (
        P("sample", None, "space", None),
        P(),
        P(),
        P(),
        P(),
        P("sample", None, "space", None),
    )
    out_specs = (
        P("sample", None, "space", None),
        P("sample", None, "space", None),
        P(),
        P(),
        P(),
        P(),
    )
    return jax.shard_map(
        per_device, mesh=mesh, in_specs=in_specs, out_specs=out_specs, check_vma=False
    )
```

```python
import math

import jax
import jax.numpy as jnp
from jax import lax
from jax.sharding import PartitionSpec as P

CH_IN = 32
CH_MID = 64
CH_OUT = 128
VOL_HEIGHT = 64
VOL_WIDTH = 16


NEAR_FIRST = (0, 1, 3, 4, 2, 7, 5, 6)

LAYOUT_SPEC = ("NCDHW", "OIDHW", "NCDHW")


def padded_2(x, sides, width):
    for axis, dim in sides:
        size, length = (lax.axis_size(axis), x.shape[dim])
        up = [(i, (i + 1) % size) for i in range(size - 1)]
        down = [(j, i) for i, j in up]
        last = lax.slice_in_dim(x, length - width, length, axis=dim)
        initial = lax.slice_in_dim(x, 0, width, axis=dim)
        before = lax.ppermute(last, axis, up)
        after = lax.ppermute(initial, axis, down)
        x = jnp.concatenate([before, x, after], axis=dim)
    return x


def from_partner(block, axis, stride):
    count = lax.axis_size(axis)
    route = []
    for low in range(count):
        high = low | 1 << stride
        if high != low and high < count:
            route += [(low, high), (high, low)]
    return lax.ppermute(block, axis, route)


def shifted(x, axis, by):
    size = lax.axis_size(axis)
    pairs = [(i, i + by) for i in range(size) if 0 <= i + by < size]
    return lax.ppermute(x, axis, pairs)


def as_sent(x):

    def short(part):
        return part.astype(jnp.bfloat16) if part.dtype == jnp.float32 else part

    return jax.tree.map(short, x)


def kernel_of(weight, channels):
    return weight.reshape(weight.shape[0], 3, 3, 3, channels).transpose(0, 4, 1, 2, 3)


def flipped(kernel):
    return jnp.flip(kernel, (2, 3, 4)).transpose(1, 0, 2, 3, 4)


def correlate(padded, kernel):
    return lax.conv_general_dilated(
        padded,
        kernel,
        (1, 1, 1),
        "VALID",
        dimension_numbers=LAYOUT_SPEC,
        preferred_element_type=jnp.float32,
    )


def pad_sides(volume, depth_pad, height_pad):
    return jnp.pad(
        volume, ((0, 0), (0, 0), (depth_pad, depth_pad), (height_pad, height_pad), (1, 1))
    )


def silu_slope(values_in):
    sigmoid_v = jax.nn.sigmoid(values_in)
    return sigmoid_v * (1.0 + values_in * (1.0 - sigmoid_v))


def upsampled(pooled_grad, slope):
    sample_count, channels, planes, rows_half, cols_half = pooled_grad.shape
    shaped = slope.reshape(sample_count, channels, planes, 2, rows_half, 2, cols_half, 2)
    return (pooled_grad[:, :, :, None, :, None, :, None] * 0.125 * shaped).reshape(slope.shape)


def weight_grad(padded, slope_grad):
    summed = lax.conv_general_dilated(
        padded,
        slope_grad,
        (1, 1, 1),
        "VALID",
        dimension_numbers=("CNDHW", "IODHW", "CNDHW"),
        preferred_element_type=jnp.float32,
    )
    out_channels, in_channels = summed.shape[:2]
    return summed.transpose(0, 2, 3, 4, 1).reshape(out_channels, 27 * in_channels)


def butterfly(pieces_all, mover, own_index, bit_levels):
    for bit_level in range(bit_levels):
        step_size = 1 << bit_level
        outer_count = pieces_all.shape[0] // (2 * step_size)
        trailing = pieces_all.shape[1:]
        grouped = pieces_all.reshape((outer_count, 2, step_size) + trailing)
        lower_half = grouped[:, 0]
        upper_half = grouped[:, 1]
        bit_set = own_index >> bit_level & 1 == 1
        kept_half = jnp.where(bit_set, upper_half, lower_half)
        sent_half = jnp.where(bit_set, lower_half, upper_half)
        arrived = mover(sent_half, bit_level)
        new_lower = jnp.where(bit_set, arrived, kept_half)
        new_upper = jnp.where(bit_set, kept_half, arrived)
        pieces_all = jnp.stack([new_lower, new_upper], axis=1).reshape(pieces_all.shape)
    return pieces_all


def slabs_to_blocks(slab, mover, own_index, block_side, bit_levels):
    sample_count, channels, planes, rows_all, row_cells = slab.shape
    rows_block = rows_all // block_side
    pieces_all = jnp.moveaxis(
        slab.reshape(sample_count, channels, planes, block_side, rows_block * row_cells), 3, 0
    )
    arrived = jnp.moveaxis(butterfly(pieces_all, mover, own_index, bit_levels), 0, 2)
    return arrived.reshape(sample_count, channels, block_side * planes, rows_block, row_cells)


def blocks_to_slabs(block, mover, own_index, block_side, bit_levels):
    sample_count, channels, planes_all, rows_block, row_cells = block.shape
    planes = planes_all // block_side
    pieces_all = jnp.moveaxis(
        block.reshape(sample_count, channels, block_side, planes, rows_block * row_cells), 2, 0
    )
    arrived = jnp.moveaxis(butterfly(pieces_all, mover, own_index, bit_levels), 0, 3)
    return arrived.reshape(sample_count, channels, planes, block_side * rows_block * row_cells)


def block_halo(block, movers, own_index, block_side):
    sample_count, channels, planes, rows_block, row_cells = block.shape
    block_column = own_index % block_side
    last_row = block[:, :, :, rows_block - 1].reshape(sample_count, channels, planes * row_cells)
    first_row = block[:, :, :, 0].reshape(sample_count, channels, planes * row_cells)
    last_row = jnp.where(block_column == block_side - 1, jnp.zeros_like(last_row), last_row)
    first_row = jnp.where(block_column == 0, jnp.zeros_like(first_row), first_row)
    from_prev = movers[0](last_row)
    from_next = movers[1](first_row)
    tall_block = jnp.concatenate(
        [
            from_prev.reshape(sample_count, channels, planes, 1, row_cells),
            block,
            from_next.reshape(sample_count, channels, planes, 1, row_cells),
        ],
        axis=3,
    )
    top_plane = tall_block[:, :, planes - 1].reshape(
        sample_count, channels, (rows_block + 2) * row_cells
    )
    bottom_plane = tall_block[:, :, 0].reshape(sample_count, channels, (rows_block + 2) * row_cells)
    from_below = movers[2](top_plane)
    from_above = movers[3](bottom_plane)
    full_block = jnp.concatenate(
        [
            from_below.reshape(sample_count, channels, 1, rows_block + 2, row_cells),
            tall_block,
            from_above.reshape(sample_count, channels, 1, rows_block + 2, row_cells),
        ],
        axis=2,
    )
    return jnp.pad(full_block, ((0, 0), (0, 0), (0, 0), (0, 0), (1, 1)))


def all_summed(parts, axes):
    flat = jnp.concatenate([part.reshape(-1) for part in parts])
    levels = []
    for axis in axes:
        for bit in range(lax.axis_size(axis).bit_length() - 1):
            levels.append((axis, bit))
    levels = [levels[i] for i in NEAR_FIRST] if len(levels) == len(NEAR_FIRST) else levels
    block = 1 << len(levels)
    total = flat.shape[0]
    current = jnp.pad(flat, (0, -total % block))
    for axis, bit in levels:
        half = current.shape[0] // 2
        upper = (lax.axis_index(axis) >> bit & 1) == 1
        kept = jnp.where(upper, current[half:], current[:half])
        sent = jnp.where(upper, current[:half], current[half:])
        pairs = [(i, i ^ 1 << bit) for i in range(lax.axis_size(axis))]
        current = kept + lax.ppermute(sent, axis, pairs)
    for axis, bit in reversed(levels):
        upper = (lax.axis_index(axis) >> bit & 1) == 1
        pairs = [(i, i ^ 1 << bit) for i in range(lax.axis_size(axis))]
        other = lax.ppermute(current, axis, pairs)
        current = jnp.where(
            upper, jnp.concatenate([other, current]), jnp.concatenate([current, other])
        )
    results, start = [], 0
    for part in parts:
        results.append(current[start : start + part.size].reshape(part.shape))
        start += part.size
    return tuple(results)


def per_device(volumes, first_weight, first_bias, second_weight, second_bias, cotangent):
    sample_count = volumes.shape[0]
    depth_cells = volumes.shape[2]
    plane_cells = volumes.shape[3]
    space_count = lax.axis_size("space")
    total_samples = sample_count * lax.axis_size("sample")
    half_height = VOL_HEIGHT // 2
    half_width = VOL_WIDTH // 2
    pooled_planes = depth_cells // 2
    grad_scale = 1.0 / math.sqrt(
        total_samples * depth_cells * space_count * VOL_HEIGHT * VOL_WIDTH / 8.0
    )
    kernel_one = kernel_of(first_weight, CH_IN)
    kernel_two = kernel_of(second_weight, CH_MID)
    haloed_in = padded_2(volumes, (("space", 2),), 1)
    padded_in = pad_sides(
        haloed_in.reshape(sample_count, CH_IN, depth_cells + 2, VOL_HEIGHT, VOL_WIDTH), 0, 1
    )
    first_pre = correlate(padded_in, kernel_one) + first_bias.reshape(1, CH_MID, 1, 1, 1)
    pooled = (
        jax.nn.silu(first_pre)
        .reshape(sample_count, CH_MID, pooled_planes, 2, half_height, 2, half_width, 2)
        .mean(axis=(3, 5, 7))
        .astype(jnp.bfloat16)
    )
    cot_cells = cotangent.reshape(sample_count, CH_OUT, pooled_planes, half_height, half_width)
    pooled_cells_count = half_height * half_width
    haloed_pool = padded_2(
        pooled.reshape(sample_count, CH_MID, pooled_planes, pooled_cells_count), (("space", 2),), 1
    )
    padded_pool = pad_sides(
        haloed_pool.reshape(sample_count, CH_MID, pooled_planes + 2, half_height, half_width), 0, 1
    )
    second_pre = correlate(padded_pool, kernel_two) + second_bias.reshape(1, CH_OUT, 1, 1, 1)
    second_grad = (cot_cells.astype(jnp.float32) * silu_slope(second_pre)).astype(jnp.bfloat16)
    haloed_second = padded_2(
        second_grad.reshape(sample_count, CH_OUT, pooled_planes, pooled_cells_count),
        (("space", 2),),
        1,
    )
    padded_grad = pad_sides(
        haloed_second.reshape(sample_count, CH_OUT, pooled_planes + 2, half_height, half_width),
        0,
        1,
    )
    pooled_grad = correlate(padded_grad, flipped(kernel_two))
    activation = (
        jax.nn.silu(second_pre)
        .astype(jnp.bfloat16)
        .reshape(sample_count, CH_OUT, pooled_planes, pooled_cells_count)
    )
    second_wgrad = weight_grad(padded_pool, second_grad)
    second_bgrad = jnp.sum(second_grad, axis=(0, 2, 3, 4), dtype=jnp.float32)
    pooled_cells = pooled_grad
    first_grad = upsampled(pooled_cells, silu_slope(first_pre)).astype(jnp.bfloat16)
    first_wgrad = weight_grad(padded_in, first_grad)
    first_bgrad = jnp.sum(first_grad, axis=(0, 2, 3, 4), dtype=jnp.float32)
    first_wgrad, first_bgrad, second_wgrad, second_bgrad = all_summed(
        (first_wgrad, first_bgrad, second_wgrad, second_bgrad), ("space", "sample")
    )
    flip_one = flipped(kernel_one)
    haloed_grad = padded_2(
        first_grad.reshape(sample_count, CH_MID, depth_cells, plane_cells), (("space", 2),), 1
    )
    input_sum = correlate(
        pad_sides(
            haloed_grad.reshape(sample_count, CH_MID, depth_cells + 2, VOL_HEIGHT, VOL_WIDTH), 0, 1
        ),
        flip_one,
    )
    input_sum = input_sum.reshape(sample_count, CH_IN, depth_cells, plane_cells)
    input_grad = input_sum.astype(jnp.bfloat16)
    return (
        activation,
        input_grad,
        first_wgrad * grad_scale,
        first_bgrad * grad_scale,
        second_wgrad * grad_scale,
        second_bgrad * grad_scale,
    )


def solution(mesh):
    in_specs = (
        P("sample", None, "space", None),
        P(),
        P(),
        P(),
        P(),
        P("sample", None, "space", None),
    )
    out_specs = (
        P("sample", None, "space", None),
        P("sample", None, "space", None),
        P(),
        P(),
        P(),
        P(),
    )
    return jax.shard_map(
        per_device, mesh=mesh, in_specs=in_specs, out_specs=out_specs, check_vma=False
    )
```
